128 devices in a mesh: leaf: 128 (over z, x, y, core).
Axes of the slice: x: 4, y: 4, z: 4, core: 2. Of those that a mesh axis runs over, the one named last changes fastest.
Arguments:
- charges: bfloat16 [8192, 16, 128], P('leaf'), may hold values from -6 to 6
- leaf_basis: bfloat16 [8192, 64, 128], P('leaf'), may hold values from -0.5 to 0.5
- leaf_up: float32 [8192, 64, 64], P('leaf'), may hold values from -0.75 to 0.75
- top_up: float32 [7, 2, 64, 64], replicated, may hold values from -0.5 to 0.5
- top_coupling: float32 [7, 2, 64, 64], replicated, may hold values from -0.75 to 0.75
- near_blocks: bfloat16 [8192, 8, 128, 128], P('leaf'), may hold values from -0.5 to 0.5
- near_list: int32 [8192, 8], P('leaf'), may hold values from 0 to 8191, as said below
- coupling_blocks: bfloat16 [131072, 64, 64], P('leaf'), may hold values from -0.75 to 0.75
- coup_source: int32 [131072], P('leaf'), may hold values from 0 to 63
- coup_device: int32 [131072, 1], P('leaf'), may hold values from 0 to 127; in each aligned block of 1024 rows (0 to 1023, 1024 to 2047, ...) at most 12 rows name the same one
- coup_box: int32 [131072], P('leaf'), may hold values from 0 to 63
Outputs:
- potential: float32 [8192, 16, 128], P('leaf')
The draws below stay inside these ranges and needn't reach their ends.
Inputs may be any that keep to these rules, and one draw needn't show every extreme that they name: near_list[b, 0] = b, and every entry lies within 64 of b. `coup_device`: the interactions held by one device name each target device at most 12 times.
All inputs are finite; a program needn't handle non-finite values.
Results may differ from the reference program's by a relative error of at most 0.003.
Values may be sent and summed in bfloat16 or wider, within the bound.
No kernel may reach another device: no remote copies, remote signals or barrier semaphores. Data moves between devices by JAX's collectives and lax.ppermute only.
A program may use at most 192 MiB of HBM per device.

```python
import math
import jax
import jax.numpy as jnp
import numpy as np
from jax import lax

P_SIZE = 128
K = 64
R = 16
NEAR = 8
TOPMAX = 7
LEAF_DEV = 64
C_DEV = 1024
LEAVES = 8192
COUPLINGS = 131072
CAP = 12
N_LEAF = 128


def draw_near_list(key, part):
    key_a, key_b = jax.random.split(jax.random.fold_in(key, 17))
    rows = jnp.arange(LEAVES, dtype=jnp.int32)[:, None]
    offsets = jax.random.randint(key_a, (LEAVES, NEAR), 1, LEAF_DEV + 1)
    signs = jax.random.randint(key_b, (LEAVES, NEAR), 0, 2) * 2 - 1
    picked = jnp.clip(rows + offsets * signs, 0, LEAVES - 1)
    column = jnp.arange(NEAR, dtype=jnp.int32)[None, :]
    return jnp.where(column == 0, rows, picked).astype(jnp.int32)


def with_ends(drawn, stream_key, smallest, high):
    longest = drawn.shape.index(max(drawn.shape))
    spots = []
    for shift in (0, 1):
        where = [jax.random.randint(jax.random.fold_in(stream_key, axis), (), 0, length) for axis, length in enumerate(drawn.shape)]
        where[longest] = (where[longest] + shift) % drawn.shape[longest]
        spots.append(tuple(where))
    return drawn.at[spots[0]].set(smallest).at[spots[1]].set(high)


def block_levels(own_key, extent, cuts, low, largest):
    def one(axis_at, shards_of):
        draws = jax.random.uniform(jax.random.fold_in(jax.random.fold_in(own_key, 6), axis_at), (shards_of,), jnp.float32, low / len(cuts), largest / len(cuts))
        return jnp.repeat(jnp.exp(draws), extent[axis_at] // shards_of).reshape((-1,) + (1,) * (len(extent) - axis_at - 1))

    gain = one(*cuts[0])
    for cut in cuts[1:]:
        gain = gain * one(*cut)
    return gain


def deal_out(own_key, own, number, rows, amount, top, reach, lean):
    order = jax.random.permutation(own_key, amount)
    packed, usual = portions_of(amount, rows * top, reach, lean, True), portions_of(amount, rows * top, reach, lean, False)
    places = jnp.arange(amount)

    def named(sizes, rotation):
        used = int((sizes > 0).sum())
        fixed = max(1, used // 4)
        passed = fixed + (places - fixed + rotation * (used - fixed)) % max(1, amount - fixed)
        return jnp.zeros((amount,), jnp.int32).at[order[jnp.where(places < fixed, places, passed)]].set(jnp.asarray(sizes, jnp.int32))

    sizes = jnp.where(number % 4 == 0, named(packed, number // 4), named(usual, number - number // 4 - 1))
    mixed = jax.random.permutation(jax.random.fold_in(own, 3), amount)
    donor, receiver = mixed[0:amount // 2 * 2:2], mixed[1:amount // 2 * 2:2]
    slack = jnp.minimum(sizes[donor] - 1, reach - sizes[receiver]) // 2
    slack = jnp.where((donor == order[0]) | (receiver == order[0]) | (sizes[receiver] == 0), 0, jnp.maximum(slack, 0))
    passed = jax.random.randint(jax.random.fold_in(own, 4), (amount // 2,), 0, 1 << 20) % (slack + 1)
    sizes = sizes.at[donor].add(-passed).at[receiver].add(passed)
    members = jnp.searchsorted(jnp.cumsum(sizes), jnp.arange(rows * top), side="right").astype(jnp.int32)
    grid = members.reshape(top, rows).T
    grid = grid[jax.random.permutation(jax.random.fold_in(own, 1), rows)]
    rotation = jax.random.randint(jax.random.fold_in(own, 2), (rows, 1), 0, top)
    return jnp.take_along_axis(grid, (jnp.arange(top)[None, :] + rotation) % top, axis=1)


def portions_of(count, total, bound, lean, full):
    loads = [(1 << 20) // math.isqrt(standing ** lean) + 1 for standing in range(1, count + 1)]
    largest = bound if full else min(bound, max(-(-total // count), total * loads[0] // sum(loads)))
    least = 1 if total - largest >= count - 1 else 0
    given, rest = [largest] + [least] * (count - 1), total - largest - least * (count - 1)
    while rest > 0:
        movable = [i for i in range(1, count) if given[i] < largest] or [i for i in range(1, count) if given[i] < bound]
        whole, remaining = sum([loads[i] for i in movable]), rest
        for i in movable:
            extra = min(bound - given[i], max(1, remaining * loads[i] // whole), rest)
            given[i] = given[i] + extra
            rest = rest - extra
    return np.array(given)


def gaussian(own_key, extent, scale, reach, cuts=(), kind=jnp.bfloat16):
    factor_of = block_levels(own_key, extent, cuts, -0.22, 0.18) if cuts else 1.0
    drawn = jax.random.normal(own_key, extent, jnp.float32) * scale * factor_of
    return jnp.minimum(jnp.maximum(drawn, -reach), reach).astype(kind)


def setup_inputs(seed: int = 0) -> dict:
    keys = jax.random.split(jax.random.key(seed), 12)
    charges = gaussian(keys[0], (LEAVES, R, P_SIZE), 1.0, 6.0, ((0, 128),))
    leaf_basis = gaussian(keys[1], (LEAVES, K, P_SIZE), P_SIZE ** -0.5, 0.5, ((0, 128),))
    leaf_up = gaussian(keys[2], (LEAVES, K, K), K ** -0.5, 0.75, ((0, 128),), jnp.float32)
    top_up = gaussian(keys[3], (TOPMAX, 2, K, K), (2 * K) ** -0.5, 0.5, (), jnp.float32)
    top_coupling = gaussian(keys[4], (TOPMAX, 2, K, K), K ** -0.5, 0.75, (), jnp.float32)
    near_blocks = gaussian(keys[5], (LEAVES, NEAR, P_SIZE, P_SIZE), P_SIZE ** -0.5, 0.5, ((0, 128),))
    near_list = draw_near_list(jax.random.fold_in(keys[11], 71), 0)
    coupling_blocks = gaussian(keys[7], (COUPLINGS, K, K), K ** -0.5, 0.75, ((0, 128),))
    coup_source = with_ends(jax.random.randint(keys[8], (COUPLINGS,), 0, LEAF_DEV), jax.random.fold_in(keys[8], 1), 0, LEAF_DEV - 1).astype(jnp.int32)
    coup_device_keys = jax.random.split(jax.random.fold_in(keys[9], 1), COUPLINGS // C_DEV)
    coup_device_turns = jax.random.permutation(jax.random.fold_in(keys[9], 3), COUPLINGS // C_DEV)
    coup_device = jax.vmap(lambda own, number: deal_out(jax.random.fold_in(keys[9], 2), own, number, C_DEV, N_LEAF, 1, CAP, 2))(coup_device_keys, coup_device_turns).reshape((COUPLINGS, 1))
    coup_box = with_ends(jax.random.randint(keys[10], (COUPLINGS,), 0, LEAF_DEV), jax.random.fold_in(keys[10], 1), 0, LEAF_DEV - 1).astype(jnp.int32)
    return dict(charges=charges, leaf_basis=leaf_basis, leaf_up=leaf_up, top_up=top_up, top_coupling=top_coupling, near_blocks=near_blocks, near_list=near_list, coupling_blocks=coupling_blocks, coup_source=coup_source, coup_device=coup_device, coup_box=coup_box)


def top_tree(boxes, top_up, top_coupling, levels):
    highest = lax.Precision.HIGHEST
    upward = boxes
    stored = []
    for level in range(levels):
        count = upward.shape[0]
        node_side = jnp.arange(count, dtype=jnp.int32) % 2
        paired = upward.reshape(count // 2, 2, upward.shape[1], upward.shape[2])
        left_node = paired[:, 0]
        right_node = paired[:, 1]
        partner = jnp.stack([right_node, left_node], axis=1).reshape(upward.shape)
        coupled = jnp.einsum('nrj,njk->nrk', partner, top_coupling[level][node_side], precision=highest)
        stored.append(coupled)
        upward = jnp.einsum('nrj,jk->nrk', left_node, top_up[level, 0], precision=highest) + jnp.einsum('nrj,jk->nrk', right_node, top_up[level, 1], precision=highest)
    local_exp = jnp.zeros_like(upward)
    for level in reversed(range(levels)):
        count = stored[level].shape[0]
        node_side = jnp.arange(count, dtype=jnp.int32) % 2
        parent = jnp.repeat(local_exp, 2, axis=0)
        local_exp = jnp.einsum('nrk,njk->nrj', parent, top_up[level][node_side], precision=highest) + stored[level]
    return local_exp


def reference(charges, leaf_basis, leaf_up, top_up, top_coupling, near_blocks, near_list, coupling_blocks, coup_source, coup_device, coup_box):
    highest = lax.Precision.HIGHEST
    levels = N_LEAF.bit_length() - 1
    skeleton = jnp.einsum('bkp,brp->brk', leaf_basis.astype(jnp.float32), charges.astype(jnp.float32), precision=highest)
    skeleton_low = skeleton.astype(jnp.bfloat16)
    lifted = jnp.einsum('brj,bjk->brk', skeleton, leaf_up, precision=highest)
    boxes = lifted.reshape(N_LEAF, LEAF_DEV, R, K).sum(axis=1)
    device_local = top_tree(boxes, top_up, top_coupling, levels)

    owner_dev = jnp.arange(COUPLINGS, dtype=jnp.int32) // C_DEV
    source_rows = owner_dev * LEAF_DEV + coup_source

    def coupling_part(operands):
        rows, blocks = operands
        picked = skeleton_low[rows].astype(jnp.float32)
        return jnp.einsum('crj,cjk->crk', picked, blocks.astype(jnp.float32), precision=highest).astype(jnp.bfloat16)

    results = lax.map(coupling_part, (source_rows.reshape(N_LEAF, C_DEV), coupling_blocks.reshape(N_LEAF, C_DEV, K, K)))
    targets = coup_device[:, 0] * LEAF_DEV + coup_box
    far = jax.ops.segment_sum(results.reshape(COUPLINGS, R, K).astype(jnp.float32), targets, num_segments=LEAVES)

    spread = jnp.repeat(device_local, LEAF_DEV, axis=0)
    leaf_local = (jnp.einsum('brk,bjk->brj', spread, leaf_up, precision=highest) + far).astype(jnp.bfloat16)

    def near_part(operands):
        rows, blocks = operands
        gathered = charges[rows].astype(jnp.float32)
        return jnp.einsum('bjrq,bjqp->brp', gathered, blocks.astype(jnp.float32), precision=highest)

    nearfield = lax.map(near_part, (near_list.reshape(N_LEAF, LEAF_DEV, NEAR), near_blocks.reshape(N_LEAF, LEAF_DEV, NEAR, P_SIZE, P_SIZE)))
    nearfield = nearfield.reshape(LEAVES, R, P_SIZE)
    farfield = jnp.einsum('brk,bkp->brp', leaf_local.astype(jnp.float32), leaf_basis.astype(jnp.float32), precision=highest)
    return farfield + nearfield
```

```python
import jax
import jax.numpy as jnp
from jax import lax
from jax.sharding import PartitionSpec as P


def padded_2(value, sides, width):
    for axis, dim in sides:
        peers, length = (lax.axis_size(axis), value.shape[dim])
        up = [(i, (i + 1) % peers) for i in range(peers - 1)]
        down = [(j, i) for i, j in up]
        last = lax.slice_in_dim(value, length - width, length, axis=dim)
        initial = lax.slice_in_dim(value, 0, width, axis=dim)
        before = lax.ppermute(last, axis, up)
        after = lax.ppermute(initial, axis, down)
        value = jnp.concatenate([before, value, after], axis=dim)
    return value


def body(
    charges,
    leaf_basis,
    leaf_up,
    top_up,
    top_coupling,
    near_blocks,
    near_list,
    coupling_blocks,
    coup_source,
    coup_device,
    coup_box,
):
    highest = lax.Precision.HIGHEST
    device_pos = lax.axis_index("leaf")
    devices = lax.axis_size("leaf")
    levels = devices.bit_length() - 1
    leaf_count = charges.shape[0]
    ranks = leaf_basis.shape[1]
    sides_rhs = charges.shape[1]
    panels = charges.shape[2]
    near_count = near_list.shape[1]
    entries = coup_source.shape[0]
    capacity = entries // devices + entries // (2 * devices)
    capacity = -(-capacity // 8) * 8
    slots = devices * capacity
    flat_width = sides_rhs * ranks

    target_dev = coup_device[:, 0]
    onehot_dev = (target_dev[:, None] == jnp.arange(devices, dtype=jnp.int32)[None, :]).astype(
        jnp.int32
    )
    slot_pos = jnp.sum((jnp.cumsum(onehot_dev, axis=0) - onehot_dev) * onehot_dev, axis=1)
    slot_flat = target_dev * capacity + slot_pos
    slot_table = (
        jnp.arange(slots, dtype=jnp.int32)[:, None] == slot_flat[None, :]
    ).astype(jnp.bfloat16)
    box_plus = (coup_box + 1).astype(jnp.bfloat16)
    box_buffer = (
        jnp.dot(slot_table, box_plus, preferred_element_type=jnp.float32).astype(jnp.int32) - 1
    )
    recv_boxes = lax.all_to_all(
        box_buffer.reshape(devices, 1, capacity), "leaf", split_axis=0, concat_axis=0, tiled=True
    )

    skeleton = jnp.einsum("bkp,brp->brk", leaf_basis, charges, preferred_element_type=jnp.float32)
    skeleton_low = skeleton.astype(jnp.bfloat16)
    own_box = jnp.einsum("brj,bjk->rk", skeleton, leaf_up, precision=highest)

    picked = skeleton_low[coup_source]
    products = jnp.einsum(
        "crj,cjk->crk", picked, coupling_blocks, preferred_element_type=jnp.float32
    ).astype(jnp.bfloat16)
    send_values = jnp.dot(
        slot_table, products.reshape(entries, flat_width), preferred_element_type=jnp.float32
    ).astype(jnp.bfloat16)
    received = lax.all_to_all(
        send_values.reshape(devices, capacity, flat_width),
        "leaf",
        split_axis=0,
        concat_axis=0,
        tiled=True,
    )

    boxes_all = lax.all_gather(own_box, "leaf", axis=0, tiled=False)
    upward = boxes_all
    ups = []
    for level in range(levels):
        ups.append(upward)
        if level + 1 < levels:
            count = upward.shape[0]
            paired = upward.reshape(count // 2, 2, sides_rhs, ranks)
            upward = jnp.einsum("nsrj,sjk->nrk", paired, top_up[level], precision=highest)
    local_exp = jnp.zeros((sides_rhs, ranks), jnp.float32)
    for level in reversed(range(levels)):
        node = device_pos >> level
        node_side = node & 1
        sibling = lax.dynamic_index_in_dim(ups[level], node ^ 1, 0, keepdims=False)
        coupled = jnp.dot(
            sibling,
            lax.dynamic_index_in_dim(top_coupling[level], node_side, 0, keepdims=False),
            precision=highest,
        )
        local_exp = (
            jnp.dot(
                local_exp,
                lax.dynamic_index_in_dim(top_up[level], node_side, 0, keepdims=False).T,
                precision=highest,
            )
            + coupled
        )

    padded = padded_2(charges, (("leaf", 0),), leaf_count)
    local_rows = near_list - (device_pos * leaf_count - leaf_count)
    gathered = padded[local_rows]
    gathered = jnp.transpose(gathered, (0, 2, 1, 3)).reshape(
        leaf_count, sides_rhs, near_count * panels
    )
    nearfield = jnp.einsum(
        "brm,bmp->brp",
        gathered,
        near_blocks.reshape(leaf_count, near_count * panels, panels),
        preferred_element_type=jnp.float32,
    )

    scatter_table = (
        recv_boxes.reshape(1, slots) == jnp.arange(leaf_count, dtype=jnp.int32)[:, None]
    ).astype(jnp.bfloat16)
    far = jnp.dot(
        scatter_table,
        received.reshape(slots, flat_width),
        preferred_element_type=jnp.float32,
    )
    far = far.reshape(leaf_count, sides_rhs, ranks)
    leaf_local = (jnp.einsum("rk,bjk->brj", local_exp, leaf_up, precision=highest) + far).astype(
        jnp.bfloat16
    )
    farfield = jnp.einsum(
        "brk,bkp->brp", leaf_local, leaf_basis, preferred_element_type=jnp.float32
    )
    return farfield + nearfield


def solution(mesh):
    return jax.shard_map(
        body,
        mesh=mesh,
        in_specs=(
            P("leaf", None, None),
            P("leaf", None, None),
            P("leaf", None, None),
            P(),
            P(),
            P("leaf", None, None, None),
            P("leaf", None),
            P("leaf", None, None),
            P("leaf"),
            P("leaf", None),
            P("leaf"),
        ),
        out_specs=P("leaf", None, None),
        check_vma=False,
    )
```

```python
import jax
import jax.numpy as jnp
from jax import lax
from jax.sharding import PartitionSpec as P


def padded_2(value, sides, width):
    for axis, dim in sides:
        peers, length = (lax.axis_size(axis), value.shape[dim])
        up = [(i, (i + 1) % peers) for i in range(peers - 1)]
        down = [(j, i) for i, j in up]
        last = lax.slice_in_dim(value, length - width, length, axis=dim)
        initial = lax.slice_in_dim(value, 0, width, axis=dim)
        before = lax.ppermute(last, axis, up)
        after = lax.ppermute(initial, axis, down)
        value = jnp.concatenate([before, value, after], axis=dim)
    return value


def body(
    charges,
    leaf_basis,
    leaf_up,
    top_up,
    top_coupling,
    near_blocks,
    near_list,
    coupling_blocks,
    coup_source,
    coup_device,
    coup_box,
):
    highest = lax.Precision.HIGHEST
    device_pos = lax.axis_index("leaf")
    devices = lax.axis_size("leaf")
    levels = devices.bit_length() - 1
    leaf_count = charges.shape[0]
    ranks = leaf_basis.shape[1]
    sides_rhs = charges.shape[1]
    panels = charges.shape[2]
    near_count = near_list.shape[1]
    entries = coup_source.shape[0]
    capacity = entries // devices + entries // (2 * devices)
    rows = -(-(capacity + 1) // 8) * 8
    flat_width = sides_rhs * ranks

    target_dev = coup_device[:, 0]
    onehot_dev = (target_dev[:, None] == jnp.arange(devices, dtype=jnp.int32)[None, :]).astype(
        jnp.int32
    )
    slot_pos = jnp.sum((jnp.cumsum(onehot_dev, axis=0) - onehot_dev) * onehot_dev, axis=1)
    slot_flat = target_dev * rows + slot_pos
    slot_table = (
        jnp.arange(devices * rows, dtype=jnp.int32)[:, None] == slot_flat[None, :]
    ).astype(jnp.bfloat16)
    box_plus = (coup_box + 1).astype(jnp.bfloat16)
    box_slots = jnp.dot(
        slot_table.reshape(devices, rows, entries)[:, :capacity, :],
        box_plus,
        preferred_element_type=jnp.float32,
    )
    lanes = -(-capacity // 128) * 128
    box_table = jnp.where(
        jnp.arange(rows, dtype=jnp.int32)[None, :, None] == capacity,
        jnp.pad(box_slots, ((0, 0), (0, lanes - capacity)))[:, None, :],
        0.0,
    ).astype(jnp.bfloat16).reshape(devices * rows, lanes)
    lane_place = (
        jnp.arange(lanes, dtype=jnp.int32)[:, None] == jnp.arange(flat_width, dtype=jnp.int32)[None, :]
    ).astype(jnp.bfloat16)

    skeleton = jnp.einsum("bkp,brp->brk", leaf_basis, charges, preferred_element_type=jnp.float32)
    skeleton_low = skeleton.astype(jnp.bfloat16)
    own_box = jnp.einsum("brj,bjk->rk", skeleton, leaf_up, precision=highest)

    source_table = (
        coup_source[:, None] == jnp.arange(leaf_count, dtype=jnp.int32)[None, :]
    ).astype(jnp.bfloat16)
    picked = jnp.einsum(
        "es,srj->erj", source_table, skeleton_low, preferred_element_type=jnp.float32
    ).astype(jnp.bfloat16)
    products = jnp.einsum(
        "crj,cjk->crk", picked, coupling_blocks, preferred_element_type=jnp.float32
    ).astype(jnp.bfloat16)
    send_values = jnp.dot(
        slot_table, products.reshape(entries, flat_width), preferred_element_type=jnp.float32
    ) + jnp.dot(box_table, lane_place, preferred_element_type=jnp.float32)
    send_values = send_values.astype(jnp.bfloat16).reshape(devices, rows, flat_width)
    received = lax.all_to_all(send_values, "leaf", split_axis=0, concat_axis=0, tiled=True)
    recv_boxes = jnp.where(
        jnp.arange(rows, dtype=jnp.int32)[None, :] < capacity,
        jnp.pad(received[:, capacity, :capacity], ((0, 0), (0, rows - capacity))).astype(jnp.int32),
        0,
    ) - 1

    boxes_all = lax.all_gather(
        jnp.concatenate([own_box, jnp.zeros_like(own_box)], axis=0), "leaf", axis=0, tiled=False
    )[:, :sides_rhs]
    upward = boxes_all
    ups = []
    for level in range(levels):
        ups.append(upward)
        if level + 1 < levels:
            count = upward.shape[0]
            paired = upward.reshape(count // 2, 2, sides_rhs, ranks)
            upward = jnp.einsum("nsrj,sjk->nrk", paired, top_up[level], precision=highest)
    local_exp = jnp.zeros((sides_rhs, ranks), jnp.float32)
    for level in reversed(range(levels)):
        node = device_pos >> level
        node_side = node & 1
        sibling = lax.dynamic_index_in_dim(ups[level], node ^ 1, 0, keepdims=False)
        coupled = jnp.dot(
            sibling,
            lax.dynamic_index_in_dim(top_coupling[level], node_side, 0, keepdims=False),
            precision=highest,
        )
        local_exp = (
            jnp.dot(
                local_exp,
                lax.dynamic_index_in_dim(top_up[level], node_side, 0, keepdims=False).T,
                precision=highest,
            )
            + coupled
        )

    padded = padded_2(charges, (("leaf", 0),), leaf_count)
    local_rows = near_list - (device_pos * leaf_count - leaf_count)
    gathered = padded[local_rows]
    gathered = jnp.transpose(gathered, (0, 2, 1, 3)).reshape(
        leaf_count, sides_rhs, near_count * panels
    )
    nearfield = jnp.einsum(
        "brm,bmp->brp",
        gathered,
        near_blocks.reshape(leaf_count, near_count * panels, panels),
        preferred_element_type=jnp.float32,
    )

    scatter_table = (
        recv_boxes.reshape(1, devices * rows) == jnp.arange(leaf_count, dtype=jnp.int32)[:, None]
    ).astype(jnp.bfloat16)
    far = jnp.dot(
        scatter_table,
        received.reshape(devices * rows, flat_width),
        preferred_element_type=jnp.float32,
    )
    far = far.reshape(leaf_count, sides_rhs, ranks)
    leaf_local = (jnp.einsum("rk,bjk->brj", local_exp, leaf_up, precision=highest) + far).astype(
        jnp.bfloat16
    )
    farfield = jnp.einsum(
        "brk,bkp->brp", leaf_local, leaf_basis, preferred_element_type=jnp.float32
    )
    return farfield + nearfield


def solution(mesh):
    return jax.shard_map(
        body,
        mesh=mesh,
        in_specs=(
            P("leaf", None, None),
            P("leaf", None, None),
            P("leaf", None, None),
            P(),
            P(),
            P("leaf", None, None, None),
            P("leaf", None),
            P("leaf", None, None),
            P("leaf"),
            P("leaf", None),
            P("leaf"),
        ),
        out_specs=P("leaf", None, None),
        check_vma=False,
    )
```

```python
import jax
import jax.numpy as jnp
from jax import lax
from jax.experimental import pallas as pl
from jax.sharding import PartitionSpec as P


def padded_2(value, sides, width):
    for axis, dim in sides:
        peers, length = (lax.axis_size(axis), value.shape[dim])
        up = [(i, (i + 1) % peers) for i in range(peers - 1)]
        down = [(j, i) for i, j in up]
        last = lax.slice_in_dim(value, length - width, length, axis=dim)
        initial = lax.slice_in_dim(value, 0, width, axis=dim)
        before = lax.ppermute(last, axis, up)
        after = lax.ppermute(initial, axis, down)
        value = jnp.concatenate([before, value, after], axis=dim)
    return value


def scatter_kernel(boxes_ref, values_ref, out_ref):
    table = (
        boxes_ref[...] == lax.broadcasted_iota(jnp.int32, (out_ref.shape[0], boxes_ref.shape[1]), 0)
    ).astype(values_ref.dtype)
    out_ref[...] = jnp.dot(table, values_ref[...], preferred_element_type=jnp.float32)


def scatter_rows(boxes, values, count):
    slots, width = values.shape
    step = 256
    return pl.pallas_call(
        scatter_kernel,
        grid=(width // step,),
        in_specs=[
            pl.BlockSpec((1, slots), lambda i: (0, 0)),
            pl.BlockSpec((slots, step), lambda i: (0, i)),
        ],
        out_specs=pl.BlockSpec((count, step), lambda i: (0, i)),
        out_shape=jax.ShapeDtypeStruct((count, width), jnp.float32),
        cost_estimate=pl.CostEstimate(
            flops=2 * count * slots * width,
            bytes_accessed=slots * width * 2 + count * width * 4 + slots * 4,
            transcendentals=0,
        ),
    )(boxes, values)


def body_inner(
    charges,
    leaf_basis,
    leaf_up,
    top_up,
    top_coupling,
    near_blocks,
    near_list,
    coupling_blocks,
    coup_source,
    coup_device,
    coup_box,
):
    highest = lax.Precision.HIGHEST
    device_pos = lax.axis_index("leaf")
    devices = lax.axis_size("leaf")
    levels = devices.bit_length() - 1
    leaf_count = charges.shape[0]
    ranks = leaf_basis.shape[1]
    sides_rhs = charges.shape[1]
    panels = charges.shape[2]
    near_count = near_list.shape[1]
    entries = coup_source.shape[0]
    capacity = entries // devices + entries // (2 * devices)
    rows = -(-(capacity + 1) // 8) * 8
    flat_width = sides_rhs * ranks

    target_dev = coup_device[:, 0]
    onehot_dev = (target_dev[:, None] == jnp.arange(devices, dtype=jnp.int32)[None, :]).astype(
        jnp.int32
    )
    slot_pos = jnp.sum((jnp.cumsum(onehot_dev, axis=0) - onehot_dev) * onehot_dev, axis=1)
    slot_flat = target_dev * rows + slot_pos
    slot_table = (
        jnp.arange(devices * rows, dtype=jnp.int32)[:, None] == slot_flat[None, :]
    ).astype(jnp.bfloat16)
    box_plus = (coup_box + 1).astype(jnp.bfloat16)
    box_slots = jnp.dot(
        slot_table.reshape(devices, rows, entries)[:, :capacity, :],
        box_plus,
        preferred_element_type=jnp.float32,
    )
    lanes = -(-capacity // 128) * 128
    box_table = jnp.where(
        jnp.arange(rows, dtype=jnp.int32)[None, :, None] == capacity,
        jnp.pad(box_slots, ((0, 0), (0, lanes - capacity)))[:, None, :],
        0.0,
    ).astype(jnp.bfloat16).reshape(devices * rows, lanes)
    lane_place = (
        jnp.arange(lanes, dtype=jnp.int32)[:, None] == jnp.arange(flat_width, dtype=jnp.int32)[None, :]
    ).astype(jnp.bfloat16)

    skeleton = jnp.einsum("bkp,brp->brk", leaf_basis, charges, preferred_element_type=jnp.float32)
    skeleton_low = skeleton.astype(jnp.bfloat16)
    own_box = jnp.einsum("brj,bjk->rk", skeleton, leaf_up, precision=highest)

    source_table = (
        coup_source[:, None] == jnp.arange(leaf_count, dtype=jnp.int32)[None, :]
    ).astype(jnp.bfloat16)
    picked = jnp.einsum(
        "es,srj->erj", source_table, skeleton_low, preferred_element_type=jnp.float32
    ).astype(jnp.bfloat16)
    products = jnp.einsum(
        "crj,cjk->crk", picked, coupling_blocks, preferred_element_type=jnp.float32
    ).astype(jnp.bfloat16)
    send_values = jnp.dot(
        slot_table, products.reshape(entries, flat_width), preferred_element_type=jnp.float32
    ) + jnp.dot(box_table, lane_place, preferred_element_type=jnp.float32)
    send_values = send_values.astype(jnp.bfloat16).reshape(devices, rows, flat_width)
    received = lax.all_to_all(send_values, "leaf", split_axis=0, concat_axis=0, tiled=True)
    recv_boxes = jnp.where(
        jnp.arange(rows, dtype=jnp.int32)[None, :] < capacity,
        jnp.pad(received[:, capacity, :capacity], ((0, 0), (0, rows - capacity))).astype(jnp.int32),
        0,
    ) - 1

    boxes_all = lax.all_gather(
        jnp.concatenate([own_box, jnp.zeros_like(own_box)], axis=0), "leaf", axis=0, tiled=False
    )[:, :sides_rhs]
    upward = boxes_all
    ups = []
    for level in range(levels):
        ups.append(upward)
        if level + 1 < levels:
            count = upward.shape[0]
            paired = upward.reshape(count // 2, 2, sides_rhs, ranks)
            upward = jnp.einsum("nsrj,sjk->nrk", paired, top_up[level], precision=highest)
    local_exp = jnp.zeros((sides_rhs, ranks), jnp.float32)
    for level in reversed(range(levels)):
        node = device_pos >> level
        node_side = node & 1
        sibling = lax.dynamic_index_in_dim(ups[level], node ^ 1, 0, keepdims=False)
        coupled = jnp.dot(
            sibling,
            lax.dynamic_index_in_dim(top_coupling[level], node_side, 0, keepdims=False),
            precision=highest,
        )
        local_exp = (
            jnp.dot(
                local_exp,
                lax.dynamic_index_in_dim(top_up[level], node_side, 0, keepdims=False).T,
                precision=highest,
            )
            + coupled
        )

    padded = padded_2(charges, (("leaf", 0),), leaf_count)
    local_rows = near_list - (device_pos * leaf_count - leaf_count)
    gathered = padded[local_rows]
    gathered = jnp.transpose(gathered, (0, 2, 1, 3)).reshape(
        leaf_count, sides_rhs, near_count * panels
    )
    nearfield = jnp.einsum(
        "brm,bmp->brp",
        gathered,
        near_blocks.reshape(leaf_count, near_count * panels, panels),
        preferred_element_type=jnp.float32,
    )
    tree_part = jnp.einsum("rk,bjk->brj", local_exp, leaf_up, precision=highest)
    nearfield, tree_part = lax.optimization_barrier((nearfield, tree_part))

    far = scatter_rows(
        recv_boxes.reshape(1, devices * rows),
        received.reshape(devices * rows, flat_width),
        leaf_count,
    )
    far = far.reshape(leaf_count, sides_rhs, ranks)
    leaf_local = (tree_part + far).astype(jnp.bfloat16)
    farfield = jnp.einsum(
        "brk,bkp->brp", leaf_local, leaf_basis, preferred_element_type=jnp.float32
    )
    return farfield + nearfield


def solution(mesh):
    return jax.shard_map(
        body_inner,
        mesh=mesh,
        in_specs=(
            P("leaf", None, None),
            P("leaf", None, None),
            P("leaf", None, None),
            P(),
            P(),
            P("leaf", None, None, None),
            P("leaf", None),
            P("leaf", None, None),
            P("leaf"),
            P("leaf", None),
            P("leaf"),
        ),
        out_specs=P("leaf", None, None),
        check_vma=False,
    )
```

```python
import jax
import jax.numpy as jnp
from jax import lax
from jax.experimental import pallas as pl
from jax.sharding import PartitionSpec as P


def padded_2(value, sides, width):
    for axis, dim in sides:
        peers, length = (lax.axis_size(axis), value.shape[dim])
        up = [(i, (i + 1) % peers) for i in range(peers - 1)]
        down = [(j, i) for i, j in up]
        last = lax.slice_in_dim(value, length - width, length, axis=dim)
        initial = lax.slice_in_dim(value, 0, width, axis=dim)
        before = lax.ppermute(last, axis, up)
        after = lax.ppermute(initial, axis, down)
        value = jnp.concatenate([before, value, after], axis=dim)
    return value


def scatter_kernel(boxes_ref, values_ref, out_ref):
    table = (
        boxes_ref[...] == lax.broadcasted_iota(jnp.int32, (out_ref.shape[0], boxes_ref.shape[1]), 0)
    ).astype(values_ref.dtype)
    out_ref[...] = jnp.dot(table, values_ref[...], preferred_element_type=jnp.float32)


def scatter_rows(boxes, values, count):
    slots, width = values.shape
    step = 512
    return pl.pallas_call(
        scatter_kernel,
        grid=(width // step,),
        in_specs=[
            pl.BlockSpec((1, slots), lambda i: (0, 0)),
            pl.BlockSpec((slots, step), lambda i: (0, i)),
        ],
        out_specs=pl.BlockSpec((count, step), lambda i: (0, i)),
        out_shape=jax.ShapeDtypeStruct((count, width), jnp.float32),
        cost_estimate=pl.CostEstimate(
            flops=2 * count * slots * width,
            bytes_accessed=slots * width * 2 + count * width * 4 + slots * 4,
            transcendentals=0,
        ),
    )(boxes, values)


def body_inner(
    charges,
    leaf_basis,
    leaf_up,
    top_up,
    top_coupling,
    near_blocks,
    near_list,
    coupling_blocks,
    coup_source,
    coup_device,
    coup_box,
):
    highest = lax.Precision.HIGHEST
    device_pos = lax.axis_index("leaf")
    devices = lax.axis_size("leaf")
    levels = devices.bit_length() - 1
    leaf_count = charges.shape[0]
    ranks = leaf_basis.shape[1]
    sides_rhs = charges.shape[1]
    panels = charges.shape[2]
    near_count = near_list.shape[1]
    entries = coup_source.shape[0]
    capacity = entries // devices + entries // (2 * devices)
    rows = -(-(capacity + 1) // 8) * 8
    flat_width = sides_rhs * ranks

    target_dev = coup_device[:, 0]
    onehot_dev = (target_dev[:, None] == jnp.arange(devices, dtype=jnp.int32)[None, :]).astype(
        jnp.int32
    )
    slot_pos = jnp.sum((jnp.cumsum(onehot_dev, axis=0) - onehot_dev) * onehot_dev, axis=1)
    slot_flat = target_dev * rows + slot_pos
    slot_table = (
        jnp.arange(devices * rows, dtype=jnp.int32)[:, None] == slot_flat[None, :]
    ).astype(jnp.bfloat16)
    box_plus = (coup_box + 1).astype(jnp.bfloat16)
    box_slots = jnp.dot(slot_table, box_plus, preferred_element_type=jnp.float32)
    box_slots = jnp.where(
        jnp.arange(rows, dtype=jnp.int32)[None, :] < capacity, box_slots.reshape(devices, rows), 0.0
    )

    skeleton = jnp.einsum("bkp,brp->brk", leaf_basis, charges, preferred_element_type=jnp.float32)
    skeleton_low = skeleton.astype(jnp.bfloat16)
    own_box = jnp.einsum("brj,bjk->rk", skeleton, leaf_up, precision=highest)

    source_table = (
        coup_source[:, None] == jnp.arange(leaf_count, dtype=jnp.int32)[None, :]
    ).astype(jnp.bfloat16)
    picked = jnp.einsum(
        "es,srj->erj", source_table, skeleton_low, preferred_element_type=jnp.float32
    ).astype(jnp.bfloat16)
    products = jnp.einsum(
        "crj,cjk->crk", picked, coupling_blocks, preferred_element_type=jnp.float32
    ).astype(jnp.bfloat16)
    send_values = jnp.dot(
        slot_table, products.reshape(entries, flat_width), preferred_element_type=jnp.float32
    ).astype(jnp.bfloat16)
    received = lax.all_to_all(
        send_values.reshape(devices, rows, flat_width),
        "leaf",
        split_axis=0,
        concat_axis=0,
        tiled=True,
    )

    gathered = lax.all_gather(
        jnp.concatenate([own_box, box_slots.reshape(-1, ranks)], axis=0), "leaf", axis=0, tiled=False
    )
    boxes_all = gathered[:, :sides_rhs]
    recv_boxes = (
        lax.dynamic_index_in_dim(
            gathered[:, sides_rhs:].reshape(devices, devices, rows), device_pos, 1, keepdims=False
        ).astype(jnp.int32)
        - 1
    )
    upward = boxes_all
    ups = []
    for level in range(levels):
        ups.append(upward)
        if level + 1 < levels:
            count = upward.shape[0]
            paired = upward.reshape(count // 2, 2, sides_rhs, ranks)
            upward = jnp.einsum("nsrj,sjk->nrk", paired, top_up[level], precision=highest)
    local_exp = jnp.zeros((sides_rhs, ranks), jnp.float32)
    for level in reversed(range(levels)):
        node = device_pos >> level
        node_side = node & 1
        sibling = lax.dynamic_index_in_dim(ups[level], node ^ 1, 0, keepdims=False)
        coupled = jnp.dot(
            sibling,
            lax.dynamic_index_in_dim(top_coupling[level], node_side, 0, keepdims=False),
            precision=highest,
        )
        local_exp = (
            jnp.dot(
                local_exp,
                lax.dynamic_index_in_dim(top_up[level], node_side, 0, keepdims=False).T,
                precision=highest,
            )
            + coupled
        )

    padded = padded_2(charges, (("leaf", 0),), leaf_count)
    local_rows = near_list - (device_pos * leaf_count - leaf_count)
    gathered = padded[local_rows]
    gathered = jnp.transpose(gathered, (0, 2, 1, 3)).reshape(
        leaf_count, sides_rhs, near_count * panels
    )
    nearfield = jnp.einsum(
        "brm,bmp->brp",
        gathered,
        near_blocks.reshape(leaf_count, near_count * panels, panels),
        preferred_element_type=jnp.float32,
    )
    tree_part = jnp.einsum("rk,bjk->brj", local_exp, leaf_up, precision=highest)
    nearfield, tree_part = lax.optimization_barrier((nearfield, tree_part))

    far = scatter_rows(
        recv_boxes.reshape(1, devices * rows),
        received.reshape(devices * rows, flat_width),
        leaf_count,
    )
    far = far.reshape(leaf_count, sides_rhs, ranks)
    leaf_local = (tree_part + far).astype(jnp.bfloat16)
    farfield = jnp.einsum(
        "brk,bkp->brp", leaf_local, leaf_basis, preferred_element_type=jnp.float32
    )
    return farfield + nearfield


def solution(mesh):
    return jax.shard_map(
        body_inner,
        mesh=mesh,
        in_specs=(
            P("leaf", None, None),
            P("leaf", None, None),
            P("leaf", None, None),
            P(),
            P(),
            P("leaf", None, None, None),
            P("leaf", None),
            P("leaf", None, None),
            P("leaf"),
            P("leaf", None),
            P("leaf"),
        ),
        out_specs=P("leaf", None, None),
        check_vma=False,
    )
```

```python
import jax
import jax.numpy as jnp
from jax import lax
from jax.experimental import pallas as pl
from jax.sharding import PartitionSpec as P


def padded_2(value, sides, width):
    for axis, dim in sides:
        peers, length = (lax.axis_size(axis), value.shape[dim])
        up = [(i, (i + 1) % peers) for i in range(peers - 1)]
        down = [(j, i) for i, j in up]
        last = lax.slice_in_dim(value, length - width, length, axis=dim)
        initial = lax.slice_in_dim(value, 0, width, axis=dim)
        before = lax.ppermute(last, axis, up)
        after = lax.ppermute(initial, axis, down)
        value = jnp.concatenate([before, value, after], axis=dim)
    return value


def scatter_kernel(boxes_ref, values_ref, out_ref):
    table = (
        boxes_ref[0] == lax.broadcasted_iota(jnp.int32, (out_ref.shape[0], boxes_ref.shape[2]), 0)
    ).astype(values_ref.dtype)
    out_ref[...] = jnp.dot(table, values_ref[...], preferred_element_type=jnp.float32)


def scatter_rows(boxes, values, count):
    parts, slots = boxes.shape
    width = values.shape[1]
    return pl.pallas_call(
        scatter_kernel,
        grid=(parts,),
        in_specs=[
            pl.BlockSpec((1, 1, slots), lambda i: (i, 0, 0)),
            pl.BlockSpec((slots, width), lambda i: (0, 0)),
        ],
        out_specs=pl.BlockSpec((count, width), lambda i: (0, i)),
        out_shape=jax.ShapeDtypeStruct((count, parts * width), jnp.float32),
        cost_estimate=pl.CostEstimate(
            flops=2 * count * slots * width * parts,
            bytes_accessed=slots * width * 2 + count * width * parts * 4 + parts * slots * 4,
            transcendentals=0,
        ),
    )(boxes.reshape(parts, 1, slots), values)


def body_inner(
    charges,
    leaf_basis,
    leaf_up,
    top_up,
    top_coupling,
    near_blocks,
    near_list,
    coupling_blocks,
    coup_source,
    coup_device,
    coup_box,
):
    highest = lax.Precision.HIGHEST
    device_pos = lax.axis_index("leaf")
    devices = lax.axis_size("leaf")
    levels = devices.bit_length() - 1
    leaf_count = charges.shape[0]
    ranks = leaf_basis.shape[1]
    sides_rhs = charges.shape[1]
    panels = charges.shape[2]
    near_count = near_list.shape[1]
    entries = coup_source.shape[0]
    capacity = entries // devices + entries // (2 * devices)
    rows = -(-(capacity + 1) // 8) * 8
    flat_width = sides_rhs * ranks

    target_dev = coup_device[:, 0]
    onehot_dev = (target_dev[:, None] == jnp.arange(devices, dtype=jnp.int32)[None, :]).astype(
        jnp.int32
    )
    slot_pos = jnp.sum((jnp.cumsum(onehot_dev, axis=0) - onehot_dev) * onehot_dev, axis=1)
    slot_flat = target_dev * rows + slot_pos
    slot_table = (
        jnp.arange(devices * rows, dtype=jnp.int32)[:, None] == slot_flat[None, :]
    ).astype(jnp.bfloat16)
    box_plus = (coup_box + 1).astype(jnp.bfloat16)
    box_slots = jnp.dot(slot_table, box_plus, preferred_element_type=jnp.float32)
    box_slots = jnp.where(
        jnp.arange(rows, dtype=jnp.int32)[None, :] < capacity, box_slots.reshape(devices, rows), 0.0
    )

    skeleton = jnp.einsum("bkp,brp->brk", leaf_basis, charges, preferred_element_type=jnp.float32)
    skeleton_low = skeleton.astype(jnp.bfloat16)
    own_box = jnp.einsum("brj,bjk->rk", skeleton, leaf_up, precision=highest)

    source_table = (
        coup_source[:, None] == jnp.arange(leaf_count, dtype=jnp.int32)[None, :]
    ).astype(jnp.bfloat16)
    picked = jnp.einsum(
        "es,srj->erj", source_table, skeleton_low, preferred_element_type=jnp.float32
    ).astype(jnp.bfloat16)
    products = jnp.einsum(
        "crj,cjk->crk", picked, coupling_blocks, preferred_element_type=jnp.float32
    ).astype(jnp.bfloat16)
    halves = 2
    slot_half = (
        (target_dev * capacity + slot_pos)[:, None] * halves
        + jnp.arange(halves, dtype=jnp.int32)[None, :]
    ).reshape(1, entries * halves)
    half_table = (
        jnp.arange(devices * capacity * halves, dtype=jnp.int32)[:, None] == slot_half
    ).astype(jnp.bfloat16)
    send_values = jnp.dot(
        half_table,
        products.reshape(entries * halves, flat_width // halves),
        preferred_element_type=jnp.float32,
    ).astype(jnp.bfloat16)
    received = lax.all_to_all(
        send_values.reshape(devices, capacity * halves, flat_width // halves),
        "leaf",
        split_axis=0,
        concat_axis=0,
        tiled=True,
    )

    gathered = lax.all_gather(
        jnp.concatenate([own_box, box_slots.reshape(-1, ranks)], axis=0), "leaf", axis=0, tiled=False
    )
    boxes_all = gathered[:, :sides_rhs]
    recv_boxes = (
        lax.dynamic_index_in_dim(
            gathered[:, sides_rhs:].reshape(devices, devices, rows), device_pos, 1, keepdims=False
        ).astype(jnp.int32)
        - 1
    )
    upward = boxes_all
    ups = []
    for level in range(levels):
        ups.append(upward)
        if level + 1 < levels:
            count = upward.shape[0]
            paired = upward.reshape(count // 2, 2, sides_rhs, ranks)
            upward = jnp.einsum("nsrj,sjk->nrk", paired, top_up[level], precision=highest)
    local_exp = jnp.zeros((sides_rhs, ranks), jnp.float32)
    for level in reversed(range(levels)):
        node = device_pos >> level
        node_side = node & 1
        sibling = lax.dynamic_index_in_dim(ups[level], node ^ 1, 0, keepdims=False)
        coupled = jnp.dot(
            sibling,
            lax.dynamic_index_in_dim(top_coupling[level], node_side, 0, keepdims=False),
            precision=highest,
        )
        local_exp = (
            jnp.dot(
                local_exp,
                lax.dynamic_index_in_dim(top_up[level], node_side, 0, keepdims=False).T,
                precision=highest,
            )
            + coupled
        )

    padded = padded_2(charges, (("leaf", 0),), leaf_count)
    local_rows = near_list - (device_pos * leaf_count - leaf_count)
    gathered = padded[local_rows]
    gathered = jnp.transpose(gathered, (0, 2, 1, 3)).reshape(
        leaf_count, sides_rhs, near_count * panels
    )
    nearfield = jnp.einsum(
        "brm,bmp->brp",
        gathered,
        near_blocks.reshape(leaf_count, near_count * panels, panels),
        preferred_element_type=jnp.float32,
    )
    tree_part = jnp.einsum("rk,bjk->brj", local_exp, leaf_up, precision=highest)
    nearfield, tree_part = lax.optimization_barrier((nearfield, tree_part))

    slot_boxes = recv_boxes[:, :capacity].reshape(devices * capacity, 1)
    half_boxes = jnp.where(
        jnp.arange(halves, dtype=jnp.int32)[:, None, None]
        == jnp.arange(halves, dtype=jnp.int32)[None, None, :],
        slot_boxes[None, :, :],
        -1,
    ).reshape(halves, devices * capacity * halves)
    far = scatter_rows(
        half_boxes,
        received.reshape(devices * capacity * halves, flat_width // halves),
        leaf_count,
    )
    far = far.reshape(leaf_count, sides_rhs, ranks)
    leaf_local = (tree_part + far).astype(jnp.bfloat16)
    farfield = jnp.einsum(
        "brk,bkp->brp", leaf_local, leaf_basis, preferred_element_type=jnp.float32
    )
    return farfield + nearfield


def solution(mesh):
    return jax.shard_map(
        body_inner,
        mesh=mesh,
        in_specs=(
            P("leaf", None, None),
            P("leaf", None, None),
            P("leaf", None, None),
            P(),
            P(),
            P("leaf", None, None, None),
            P("leaf", None),
            P("leaf", None, None),
            P("leaf"),
            P("leaf", None),
            P("leaf"),
        ),
        out_specs=P("leaf", None, None),
        check_vma=False,
    )
```

```python
import jax
import jax.numpy as jnp
from jax import lax
from jax.experimental import pallas as pl
from jax.experimental.pallas import tpu as pltpu
from jax.sharding import PartitionSpec as P


def padded_2(value, sides, width):
    for axis, dim in sides:
        peers, length = (lax.axis_size(axis), value.shape[dim])
        up = [(i, (i + 1) % peers) for i in range(peers - 1)]
        down = [(j, i) for i, j in up]
        last = lax.slice_in_dim(value, length - width, length, axis=dim)
        initial = lax.slice_in_dim(value, 0, width, axis=dim)
        before = lax.ppermute(last, axis, up)
        after = lax.ppermute(initial, axis, down)
        value = jnp.concatenate([before, value, after], axis=dim)
    return value


def scatter_kernel(boxes_ref, values_ref, out_ref):
    table = (
        boxes_ref[...] == lax.broadcasted_iota(jnp.int32, (out_ref.shape[0], boxes_ref.shape[1]), 0)
    ).astype(values_ref.dtype)
    out_ref[...] = jnp.dot(table, values_ref[...], preferred_element_type=jnp.float32)


def scatter_rows(boxes, values, count):
    slots, width = values.shape
    step = 512
    return pl.pallas_call(
        scatter_kernel,
        grid=(width // step,),
        in_specs=[
            pl.BlockSpec((1, slots), lambda i: (0, 0)),
            pl.BlockSpec((slots, step), lambda i: (0, i)),
        ],
        out_specs=pl.BlockSpec((count, step), lambda i: (0, i)),
        out_shape=jax.ShapeDtypeStruct((count, width), jnp.float32),
        cost_estimate=pl.CostEstimate(
            flops=2 * count * slots * width,
            bytes_accessed=slots * width * 2 + count * width * 4 + slots * 4,
            transcendentals=0,
        ),
    )(boxes, values)


def pick_kernel(source_ref, table_ref, out_ref):
    def row(e, carry):
        out_ref[e] = table_ref[source_ref[e]]
        return carry

    lax.fori_loop(0, out_ref.shape[0], row, 0, unroll=8)


def pick_rows(table, source):
    entries = source.shape[0]
    return pl.pallas_call(
        pick_kernel,
        grid_spec=pltpu.PrefetchScalarGridSpec(
            num_scalar_prefetch=1,
            grid=(1,),
            in_specs=[pl.BlockSpec(table.shape, lambda i, src: (0, 0, 0))],
            out_specs=pl.BlockSpec((entries,) + table.shape[1:], lambda i, src: (0, 0, 0)),
        ),
        out_shape=jax.ShapeDtypeStruct((entries,) + table.shape[1:], table.dtype),
    )(source, table)


def body_inner(
    charges,
    leaf_basis,
    leaf_up,
    top_up,
    top_coupling,
    near_blocks,
    near_list,
    coupling_blocks,
    coup_source,
    coup_device,
    coup_box,
):
    highest = lax.Precision.HIGHEST
    device_pos = lax.axis_index("leaf")
    devices = lax.axis_size("leaf")
    levels = devices.bit_length() - 1
    leaf_count = charges.shape[0]
    ranks = leaf_basis.shape[1]
    sides_rhs = charges.shape[1]
    panels = charges.shape[2]
    near_count = near_list.shape[1]
    entries = coup_source.shape[0]
    capacity = entries // devices + entries // (2 * devices)
    rows = -(-(capacity + 1) // 8) * 8
    flat_width = sides_rhs * ranks

    target_dev = coup_device[:, 0]
    onehot_dev = (target_dev[:, None] == jnp.arange(devices, dtype=jnp.int32)[None, :]).astype(
        jnp.int32
    )
    slot_pos = jnp.sum((jnp.cumsum(onehot_dev, axis=0) - onehot_dev) * onehot_dev, axis=1)
    slot_flat = target_dev * rows + slot_pos
    slot_table = (
        jnp.arange(devices * rows, dtype=jnp.int32)[:, None] == slot_flat[None, :]
    ).astype(jnp.bfloat16)
    box_plus = (coup_box + 1).astype(jnp.bfloat16)
    box_slots = jnp.dot(slot_table, box_plus, preferred_element_type=jnp.float32)
    box_slots = jnp.where(
        jnp.arange(rows, dtype=jnp.int32)[None, :] < capacity, box_slots.reshape(devices, rows), 0.0
    )

    skeleton = jnp.einsum("bkp,brp->brk", leaf_basis, charges, preferred_element_type=jnp.float32)
    skeleton_low = skeleton.astype(jnp.bfloat16)
    own_box = jnp.einsum("brj,bjk->rk", skeleton, leaf_up, precision=highest)

    picked = pick_rows(skeleton_low, coup_source)
    products = jnp.einsum(
        "crj,cjk->crk", picked, coupling_blocks, preferred_element_type=jnp.float32
    ).astype(jnp.bfloat16)
    send_values = jnp.dot(
        slot_table, products.reshape(entries, flat_width), preferred_element_type=jnp.float32
    ).astype(jnp.bfloat16)
    received = lax.all_to_all(
        send_values.reshape(devices, rows, flat_width),
        "leaf",
        split_axis=0,
        concat_axis=0,
        tiled=True,
    )

    gathered = lax.all_gather(
        jnp.concatenate([own_box, box_slots.reshape(-1, ranks)], axis=0), "leaf", axis=0, tiled=False
    )
    boxes_all = gathered[:, :sides_rhs]
    recv_boxes = (
        lax.dynamic_index_in_dim(
            gathered[:, sides_rhs:].reshape(devices, devices, rows), device_pos, 1, keepdims=False
        ).astype(jnp.int32)
        - 1
    )
    upward = boxes_all
    ups = []
    for level in range(levels):
        ups.append(upward)
        if level + 1 < levels:
            count = upward.shape[0]
            paired = upward.reshape(count // 2, 2, sides_rhs, ranks)
            upward = jnp.einsum("nsrj,sjk->nrk", paired, top_up[level], precision=highest)
    local_exp = jnp.zeros((sides_rhs, ranks), jnp.float32)
    for level in reversed(range(levels)):
        node = device_pos >> level
        node_side = node & 1
        sibling = lax.dynamic_index_in_dim(ups[level], node ^ 1, 0, keepdims=False)
        coupled = jnp.dot(
            sibling,
            lax.dynamic_index_in_dim(top_coupling[level], node_side, 0, keepdims=False),
            precision=highest,
        )
        local_exp = (
            jnp.dot(
                local_exp,
                lax.dynamic_index_in_dim(top_up[level], node_side, 0, keepdims=False).T,
                precision=highest,
            )
            + coupled
        )

    padded = padded_2(charges, (("leaf", 0),), leaf_count)
    local_rows = near_list - (device_pos * leaf_count - leaf_count)
    gathered = padded[local_rows]
    gathered = jnp.transpose(gathered, (0, 2, 1, 3)).reshape(
        leaf_count, sides_rhs, near_count * panels
    )
    nearfield = jnp.einsum(
        "brm,bmp->brp",
        gathered,
        near_blocks.reshape(leaf_count, near_count * panels, panels),
        preferred_element_type=jnp.float32,
    )
    tree_part = jnp.einsum("rk,bjk->brj", local_exp, leaf_up, precision=highest)
    nearfield, tree_part = lax.optimization_barrier((nearfield, tree_part))

    far = scatter_rows(
        recv_boxes.reshape(1, devices * rows),
        received.reshape(devices * rows, flat_width),
        leaf_count,
    )
    far = far.reshape(leaf_count, sides_rhs, ranks)
    leaf_local = (tree_part + far).astype(jnp.bfloat16)
    farfield = jnp.einsum(
        "brk,bkp->brp", leaf_local, leaf_basis, preferred_element_type=jnp.float32
    )
    return farfield + nearfield


def solution(mesh):
    return jax.shard_map(
        body_inner,
        mesh=mesh,
        in_specs=(
            P("leaf", None, None),
            P("leaf", None, None),
            P("leaf", None, None),
            P(),
            P(),
            P("leaf", None, None, None),
            P("leaf", None),
            P("leaf", None, None),
            P("leaf"),
            P("leaf", None),
            P("leaf"),
        ),
        out_specs=P("leaf", None, None),
        check_vma=False,
    )
```

```python
import jax
import jax.numpy as jnp
from jax import lax
from jax.experimental import pallas as pl
from jax.experimental.pallas import tpu as pltpu
from jax.sharding import PartitionSpec as P


def padded_2(value, sides, width):
    for axis, dim in sides:
        peers, length = (lax.axis_size(axis), value.shape[dim])
        up = [(i, (i + 1) % peers) for i in range(peers - 1)]
        down = [(j, i) for i, j in up]
        last = lax.slice_in_dim(value, length - width, length, axis=dim)
        initial = lax.slice_in_dim(value, 0, width, axis=dim)
        before = lax.ppermute(last, axis, up)
        after = lax.ppermute(initial, axis, down)
        value = jnp.concatenate([before, value, after], axis=dim)
    return value


def scatter_kernel(boxes_ref, values_ref, out_ref):
    table = (
        boxes_ref[...] == lax.broadcasted_iota(jnp.int32, (out_ref.shape[0], boxes_ref.shape[1]), 0)
    ).astype(values_ref.dtype)
    out_ref[...] = jnp.dot(table, values_ref[...], preferred_element_type=jnp.float32)


def scatter_rows(boxes, values, count):
    slots, width = values.shape
    step = 512
    return pl.pallas_call(
        scatter_kernel,
        grid=(width // step,),
        in_specs=[
            pl.BlockSpec((1, slots), lambda i: (0, 0)),
            pl.BlockSpec((slots, step), lambda i: (0, i)),
        ],
        out_specs=pl.BlockSpec((count, step), lambda i: (0, i)),
        out_shape=jax.ShapeDtypeStruct((count, width), jnp.float32),
        cost_estimate=pl.CostEstimate(
            flops=2 * count * slots * width,
            bytes_accessed=slots * width * 2 + count * width * 4 + slots * 4,
            transcendentals=0,
        ),
    )(boxes, values)


def pick_kernel(source_ref, table_ref, out_ref):
    def row(e, carry):
        out_ref[e] = table_ref[source_ref[e]]
        return carry

    lax.fori_loop(0, out_ref.shape[0], row, 0, unroll=8)


def pick_rows(table, source):
    entries = source.shape[0]
    return pl.pallas_call(
        pick_kernel,
        grid_spec=pltpu.PrefetchScalarGridSpec(
            num_scalar_prefetch=1,
            grid=(1,),
            in_specs=[pl.BlockSpec(table.shape, lambda i, src: (0, 0, 0))],
            out_specs=pl.BlockSpec((entries,) + table.shape[1:], lambda i, src: (0, 0, 0)),
        ),
        out_shape=jax.ShapeDtypeStruct((entries,) + table.shape[1:], table.dtype),
    )(source, table)


def body_inner(
    charges,
    leaf_basis,
    leaf_up,
    top_up,
    top_coupling,
    near_blocks,
    near_list,
    coupling_blocks,
    coup_source,
    coup_device,
    coup_box,
):
    highest = lax.Precision.HIGHEST
    device_pos = lax.axis_index("leaf")
    devices = lax.axis_size("leaf")
    levels = devices.bit_length() - 1
    leaf_count = charges.shape[0]
    ranks = leaf_basis.shape[1]
    sides_rhs = charges.shape[1]
    panels = charges.shape[2]
    near_count = near_list.shape[1]
    entries = coup_source.shape[0]
    capacity = entries // devices + entries // (2 * devices)
    rows = -(-(capacity + 1) // 8) * 8
    flat_width = sides_rhs * ranks

    target_dev = coup_device[:, 0]
    onehot_dev = (target_dev[:, None] == jnp.arange(devices, dtype=jnp.int32)[None, :]).astype(
        jnp.bfloat16
    )
    earlier = (
        jnp.arange(entries, dtype=jnp.int32)[:, None] > jnp.arange(entries, dtype=jnp.int32)[None, :]
    ).astype(jnp.bfloat16)
    prefix = jnp.dot(earlier, onehot_dev, preferred_element_type=jnp.float32)
    slot_pos = jnp.sum(prefix * onehot_dev.astype(jnp.float32), axis=1).astype(jnp.int32)
    slot_flat = target_dev * rows + slot_pos
    slot_table = (
        jnp.arange(devices * rows, dtype=jnp.int32)[:, None] == slot_flat[None, :]
    ).astype(jnp.bfloat16)
    box_plus = (coup_box + 1).astype(jnp.bfloat16)
    box_slots = jnp.dot(slot_table, box_plus, preferred_element_type=jnp.float32)
    box_slots = jnp.where(
        jnp.arange(rows, dtype=jnp.int32)[None, :] < capacity, box_slots.reshape(devices, rows), 0.0
    )

    skeleton = jnp.einsum("bkp,brp->brk", leaf_basis, charges, preferred_element_type=jnp.float32)
    skeleton_low = skeleton.astype(jnp.bfloat16)
    own_box = jnp.einsum("brj,bjk->rk", skeleton, leaf_up, precision=highest)

    picked = pick_rows(skeleton_low, coup_source)
    products = jnp.einsum(
        "crj,cjk->crk", picked, coupling_blocks, preferred_element_type=jnp.float32
    ).astype(jnp.bfloat16)
    send_values = jnp.dot(
        slot_table, products.reshape(entries, flat_width), preferred_element_type=jnp.float32
    ).astype(jnp.bfloat16)
    received = lax.all_to_all(
        send_values.reshape(devices, rows, flat_width),
        "leaf",
        split_axis=0,
        concat_axis=0,
        tiled=True,
    )

    gathered = lax.all_gather(
        jnp.concatenate([own_box, box_slots.reshape(-1, ranks)], axis=0), "leaf", axis=0, tiled=False
    )
    boxes_all = gathered[:, :sides_rhs]
    recv_boxes = (
        lax.dynamic_index_in_dim(
            gathered[:, sides_rhs:].reshape(devices, devices, rows), device_pos, 1, keepdims=False
        ).astype(jnp.int32)
        - 1
    )
    upward = boxes_all
    ups = []
    for level in range(levels):
        ups.append(upward)
        if level + 1 < levels:
            count = upward.shape[0]
            paired = upward.reshape(count // 2, 2, sides_rhs, ranks)
            upward = jnp.einsum("nsrj,sjk->nrk", paired, top_up[level], precision=highest)
    local_exp = jnp.zeros((sides_rhs, ranks), jnp.float32)
    for level in reversed(range(levels)):
        node = device_pos >> level
        node_side = node & 1
        sibling = lax.dynamic_index_in_dim(ups[level], node ^ 1, 0, keepdims=False)
        coupled = jnp.dot(
            sibling,
            lax.dynamic_index_in_dim(top_coupling[level], node_side, 0, keepdims=False),
            precision=highest,
        )
        local_exp = (
            jnp.dot(
                local_exp,
                lax.dynamic_index_in_dim(top_up[level], node_side, 0, keepdims=False).T,
                precision=highest,
            )
            + coupled
        )

    padded = padded_2(charges, (("leaf", 0),), leaf_count)
    local_rows = near_list - (device_pos * leaf_count - leaf_count)
    gathered = padded[local_rows]
    gathered = jnp.transpose(gathered, (0, 2, 1, 3)).reshape(
        leaf_count, sides_rhs, near_count * panels
    )
    nearfield = jnp.einsum(
        "brm,bmp->brp",
        gathered,
        near_blocks.reshape(leaf_count, near_count * panels, panels),
        preferred_element_type=jnp.float32,
    )
    tree_part = jnp.einsum("rk,bjk->brj", local_exp, leaf_up, precision=highest)
    nearfield, tree_part = lax.optimization_barrier((nearfield, tree_part))

    far = scatter_rows(
        recv_boxes.reshape(1, devices * rows),
        received.reshape(devices * rows, flat_width),
        leaf_count,
    )
    far = far.reshape(leaf_count, sides_rhs, ranks)
    leaf_local = (tree_part + far).astype(jnp.bfloat16)
    farfield = jnp.einsum(
        "brk,bkp->brp", leaf_local, leaf_basis, preferred_element_type=jnp.float32
    )
    return farfield + nearfield


def solution(mesh):
    return jax.shard_map(
        body_inner,
        mesh=mesh,
        in_specs=(
            P("leaf", None, None),
            P("leaf", None, None),
            P("leaf", None, None),
            P(),
            P(),
            P("leaf", None, None, None),
            P("leaf", None),
            P("leaf", None, None),
            P("leaf"),
            P("leaf", None),
            P("leaf"),
        ),
        out_specs=P("leaf", None, None),
        check_vma=False,
    )
```

```python
import jax
import jax.numpy as jnp
from jax import lax
from jax.experimental import pallas as pl
from jax.experimental.pallas import tpu as pltpu
from jax.sharding import PartitionSpec as P


def padded_2(value, sides, width):
    for axis, dim in sides:
        peers, length = (lax.axis_size(axis), value.shape[dim])
        up = [(i, (i + 1) % peers) for i in range(peers - 1)]
        down = [(j, i) for i, j in up]
        last = lax.slice_in_dim(value, length - width, length, axis=dim)
        initial = lax.slice_in_dim(value, 0, width, axis=dim)
        before = lax.ppermute(last, axis, up)
        after = lax.ppermute(initial, axis, down)
        value = jnp.concatenate([before, value, after], axis=dim)
    return value


def scatter_kernel(boxes_ref, values_ref, base_ref, out_ref):
    table = (
        boxes_ref[...] == lax.broadcasted_iota(jnp.int32, (out_ref.shape[0], boxes_ref.shape[1]), 0)
    ).astype(values_ref.dtype)
    total = base_ref[...] + jnp.dot(table, values_ref[...], preferred_element_type=jnp.float32)
    out_ref[...] = total.astype(out_ref.dtype)


def scatter_rows(boxes, values, base):
    slots, width = values.shape
    count = base.shape[0]
    step = 512
    return pl.pallas_call(
        scatter_kernel,
        grid=(width // step,),
        in_specs=[
            pl.BlockSpec((1, slots), lambda i: (0, 0)),
            pl.BlockSpec((slots, step), lambda i: (0, i)),
            pl.BlockSpec((count, step), lambda i: (0, i)),
        ],
        out_specs=pl.BlockSpec((count, step), lambda i: (0, i)),
        out_shape=jax.ShapeDtypeStruct((count, width), jnp.bfloat16),
        cost_estimate=pl.CostEstimate(
            flops=2 * count * slots * width,
            bytes_accessed=slots * width * 2 + count * width * 6 + slots * 4,
            transcendentals=0,
        ),
    )(boxes, values, base)


def pick_kernel(source_ref, table_ref, out_ref):
    def row(e, carry):
        out_ref[e] = table_ref[source_ref[e]]
        return carry

    lax.fori_loop(0, out_ref.shape[0], row, 0, unroll=8)


def pick_rows(table, source):
    entries = source.shape[0]
    return pl.pallas_call(
        pick_kernel,
        grid_spec=pltpu.PrefetchScalarGridSpec(
            num_scalar_prefetch=1,
            grid=(1,),
            in_specs=[pl.BlockSpec(table.shape, lambda i, src: (0, 0, 0))],
            out_specs=pl.BlockSpec((entries,) + table.shape[1:], lambda i, src: (0, 0, 0)),
        ),
        out_shape=jax.ShapeDtypeStruct((entries,) + table.shape[1:], table.dtype),
    )(source, table)


def body_inner(
    charges,
    leaf_basis,
    leaf_up,
    top_up,
    top_coupling,
    near_blocks,
    near_list,
    coupling_blocks,
    coup_source,
    coup_device,
    coup_box,
):
    highest = lax.Precision.HIGHEST
    device_pos = lax.axis_index("leaf")
    devices = lax.axis_size("leaf")
    levels = devices.bit_length() - 1
    leaf_count = charges.shape[0]
    ranks = leaf_basis.shape[1]
    sides_rhs = charges.shape[1]
    panels = charges.shape[2]
    near_count = near_list.shape[1]
    entries = coup_source.shape[0]
    capacity = entries // devices + entries // (2 * devices)
    rows = -(-(capacity + 1) // 8) * 8
    flat_width = sides_rhs * ranks

    target_dev = coup_device[:, 0]
    onehot_dev = (target_dev[:, None] == jnp.arange(devices, dtype=jnp.int32)[None, :]).astype(
        jnp.bfloat16
    )
    earlier = (
        jnp.arange(entries, dtype=jnp.int32)[:, None] > jnp.arange(entries, dtype=jnp.int32)[None, :]
    ).astype(jnp.bfloat16)
    prefix = jnp.dot(earlier, onehot_dev, preferred_element_type=jnp.float32)
    slot_pos = jnp.sum(prefix * onehot_dev.astype(jnp.float32), axis=1).astype(jnp.int32)
    slot_flat = target_dev * rows + slot_pos
    slot_table = (
        jnp.arange(devices * rows, dtype=jnp.int32)[:, None] == slot_flat[None, :]
    ).astype(jnp.bfloat16)
    box_plus = (coup_box + 1).astype(jnp.bfloat16)
    box_slots = jnp.dot(slot_table, box_plus, preferred_element_type=jnp.float32)
    box_slots = jnp.where(
        jnp.arange(rows, dtype=jnp.int32)[None, :] < capacity, box_slots.reshape(devices, rows), 0.0
    )

    skeleton = jnp.einsum("bkp,brp->brk", leaf_basis, charges, preferred_element_type=jnp.float32)
    skeleton_low = skeleton.astype(jnp.bfloat16)
    own_box = jnp.einsum("brj,bjk->rk", skeleton, leaf_up, precision=highest)

    picked = pick_rows(skeleton_low, coup_source)
    products = jnp.einsum(
        "crj,cjk->crk", picked, coupling_blocks, preferred_element_type=jnp.float32
    ).astype(jnp.bfloat16)
    send_values = jnp.dot(
        slot_table, products.reshape(entries, flat_width), preferred_element_type=jnp.float32
    ).astype(jnp.bfloat16)
    received = lax.all_to_all(
        send_values.reshape(devices, rows, flat_width),
        "leaf",
        split_axis=0,
        concat_axis=0,
        tiled=True,
    )

    gathered = lax.all_gather(
        jnp.concatenate([own_box, box_slots.reshape(-1, ranks)], axis=0), "leaf", axis=0, tiled=False
    )
    boxes_all = gathered[:, :sides_rhs]
    recv_boxes = (
        lax.dynamic_index_in_dim(
            gathered[:, sides_rhs:].reshape(devices, devices, rows), device_pos, 1, keepdims=False
        ).astype(jnp.int32)
        - 1
    )
    upward = boxes_all
    ups = []
    for level in range(levels):
        ups.append(upward)
        if level + 1 < levels:
            count = upward.shape[0]
            paired = upward.reshape(count // 2, 2, sides_rhs, ranks)
            upward = jnp.einsum("nsrj,sjk->nrk", paired, top_up[level], precision=highest)
    local_exp = jnp.zeros((sides_rhs, ranks), jnp.float32)
    for level in reversed(range(levels)):
        node = device_pos >> level
        node_side = node & 1
        sibling = lax.dynamic_index_in_dim(ups[level], node ^ 1, 0, keepdims=False)
        coupled = jnp.dot(
            sibling,
            lax.dynamic_index_in_dim(top_coupling[level], node_side, 0, keepdims=False),
            precision=highest,
        )
        local_exp = (
            jnp.dot(
                local_exp,
                lax.dynamic_index_in_dim(top_up[level], node_side, 0, keepdims=False).T,
                precision=highest,
            )
            + coupled
        )

    padded = padded_2(charges, (("leaf", 0),), leaf_count)
    local_rows = near_list - (device_pos * leaf_count - leaf_count)
    gathered = padded[local_rows]
    gathered = jnp.transpose(gathered, (0, 2, 1, 3)).reshape(
        leaf_count, sides_rhs, near_count * panels
    )
    nearfield = jnp.einsum(
        "brm,bmp->brp",
        gathered,
        near_blocks.reshape(leaf_count, near_count * panels, panels),
        preferred_element_type=jnp.float32,
    )
    tree_part = jnp.einsum("rk,bjk->brj", local_exp, leaf_up, precision=highest)
    tree_part = tree_part.reshape(leaf_count, flat_width)
    nearfield, tree_part = lax.optimization_barrier((nearfield, tree_part))

    leaf_local = scatter_rows(
        recv_boxes.reshape(1, devices * rows),
        received.reshape(devices * rows, flat_width),
        tree_part.reshape(leaf_count, flat_width),
    ).reshape(leaf_count, sides_rhs, ranks)
    farfield = jnp.einsum(
        "brk,bkp->brp", leaf_local, leaf_basis, preferred_element_type=jnp.float32
    )
    return farfield + nearfield


def solution(mesh):
    return jax.shard_map(
        body_inner,
        mesh=mesh,
        in_specs=(
            P("leaf", None, None),
            P("leaf", None, None),
            P("leaf", None, None),
            P(),
            P(),
            P("leaf", None, None, None),
            P("leaf", None),
            P("leaf", None, None),
            P("leaf"),
            P("leaf", None),
            P("leaf"),
        ),
        out_specs=P("leaf", None, None),
        check_vma=False,
    )
```
